128 devices in a mesh: row: 8 (over z, core), col: 8 (over y_lo, x), dep: 2 (over y_hi).
Axes of the slice: x: 4, y: 4 (y_hi: 2, y_lo: 2; y = y_hi * 2 + y_lo), z: 4, core: 2. Of those that a mesh axis runs over, the one named last changes fastest.
Arguments:
- tokens: bfloat16 [2048, 8192], P(('dep', 'col'), 'row'), may hold values from -6 to 6
- gate_weight: bfloat16 [8192, 14336], P('row', 'col'), may hold values from -0.0625 to 0.0625
- up_weight: bfloat16 [8192, 14336], P('row', 'col'), may hold values from -0.0625 to 0.0625
- cotangent: bfloat16 [2048, 14336], P(('dep', 'row'), 'col'), may hold values from -6 to 6
Outputs:
- hidden: bfloat16 [2048, 14336], P(('dep', 'row'), 'col')
- grad_tokens: bfloat16 [2048, 8192], P(('dep', 'col'), 'row')
- grad_gate_weight: bfloat16 [8192, 14336], P('row', ('col', 'dep'))
- grad_up_weight: bfloat16 [8192, 14336], P('row', ('col', 'dep'))
The draws below stay inside these ranges and needn't reach their ends.
All inputs are finite; a program needn't handle non-finite values.
Results may differ from the reference program's by a relative error of at most 0.02.
Values may be sent and summed in bfloat16 or wider, within the bound.
No kernel may reach another device: no remote copies, remote signals or barrier semaphores. Data moves between devices by JAX's collectives and lax.ppermute only.
A program may use at most 128 MiB of HBM per device.

```python
import jax
import jax.numpy as jnp
from jax import lax

D = 8192
FF = 14336
SLICE = 1024
TOKENS = 2048
N_ROW = 8
N_COL = 8
N_DEP = 2


def level_of(key, dims, cuts, least, largest):
    level, own = 1.0, jax.random.fold_in(key, 6)
    for axis_at, parts in cuts:
        steps = jnp.exp(jax.random.uniform(jax.random.fold_in(own, axis_at), (parts,), jnp.float32, least / len(cuts), largest / len(cuts)))
        level = level * jnp.repeat(steps, dims[axis_at] // parts).reshape([-1 if axis == axis_at else 1 for axis in range(len(dims))])
    return level


def bell_draw(stream_key, dims, width, reach, cuts=(), kind=jnp.bfloat16):
    factor_of = level_of(stream_key, dims, cuts, -0.22, 0.18) if cuts else 1.0
    array = jax.random.normal(stream_key, dims, jnp.float32) * width * factor_of
    return jnp.minimum(jnp.maximum(array, -reach), reach).astype(kind)


def setup_inputs(seed: int = 0) -> dict:
    arg_keys = jax.random.split(jax.random.key(seed), 5)
    return {
        "tokens": bell_draw(arg_keys[0], (TOKENS, D), 1.0, 6.0, ((0, 16), (1, 8))),
        "gate_weight": bell_draw(arg_keys[1], (D, FF), D ** -0.5, 0.0625, ((0, 8), (1, 8))),
        "up_weight": bell_draw(arg_keys[2], (D, FF), D ** -0.5, 0.0625, ((0, 8), (1, 8))),
        "cotangent": bell_draw(arg_keys[3], (TOKENS, FF), 1.0, 6.0, ((0, 16), (1, 8))),
    }


def rounded(value):
    return lax.optimization_barrier(value.astype(jnp.bfloat16)).astype(jnp.float32)


def reference(tokens, gate_weight, up_weight, cotangent):
    feat_block = D // N_ROW
    gate = jnp.zeros((TOKENS, FF), jnp.float32)
    up = jnp.zeros((TOKENS, FF), jnp.float32)
    for index in range(N_ROW):
        lower = index * feat_block
        rows = tokens[:, lower:lower + feat_block]
        gate = gate + rounded(jnp.dot(rows, gate_weight[lower:lower + feat_block], preferred_element_type=jnp.float32))
        up = up + rounded(jnp.dot(rows, up_weight[lower:lower + feat_block], preferred_element_type=jnp.float32))
    sigma = jax.nn.sigmoid(gate)
    active = gate * sigma
    hidden = (active * up).astype(jnp.bfloat16)
    upstream = cotangent.astype(jnp.float32)
    grad_gate = (upstream * up * sigma * (1.0 + gate * (1.0 - sigma))).astype(jnp.bfloat16)
    grad_up = (upstream * active).astype(jnp.bfloat16)
    hid_block = FF // N_COL
    grad_tokens = jnp.zeros((TOKENS, D), jnp.float32)
    for index in range(N_COL):
        lower = index * hid_block
        term = jnp.dot(grad_gate[:, lower:lower + hid_block], gate_weight[:, lower:lower + hid_block].T, preferred_element_type=jnp.float32)
        term = term + jnp.dot(grad_up[:, lower:lower + hid_block], up_weight[:, lower:lower + hid_block].T, preferred_element_type=jnp.float32)
        grad_tokens = grad_tokens + rounded(term)
    sum_gate = jnp.zeros((D, FF), jnp.float32)
    sum_up = jnp.zeros((D, FF), jnp.float32)
    for index in range(N_DEP):
        lower = index * SLICE
        rows = tokens[lower:lower + SLICE].T
        sum_gate = sum_gate + rounded(jnp.dot(rows, grad_gate[lower:lower + SLICE], preferred_element_type=jnp.float32))
        sum_up = sum_up + rounded(jnp.dot(rows, grad_up[lower:lower + SLICE], preferred_element_type=jnp.float32))
    return hidden, grad_tokens.astype(jnp.bfloat16), sum_gate.astype(jnp.bfloat16), sum_up.astype(jnp.bfloat16)
```

```python
import jax
import jax.numpy as jnp
from jax import lax
from jax.sharding import PartitionSpec as P


def weight_grad(gathered, full, dep):
    contract = (((0,), (0,)), ((), ()))
    half = full.shape[1] // 2
    other = lax.dynamic_slice_in_dim(full, (1 - dep) * half, half, axis=1)
    own = lax.dynamic_slice_in_dim(full, dep * half, half, axis=1)
    send = lax.dot_general(gathered, other, contract, preferred_element_type=jnp.float32)
    recv = lax.ppermute(send.astype(jnp.bfloat16), "dep", [(0, 1), (1, 0)])
    mine = lax.dot_general(gathered, own, contract, preferred_element_type=jnp.float32)
    total = mine.astype(jnp.bfloat16).astype(jnp.float32) + recv.astype(jnp.float32)
    return total.astype(jnp.bfloat16)


def on_device(tokens, gate_weight, up_weight, cotangent):
    width = gate_weight.shape[1]
    dep = lax.axis_index("dep")
    gathered = lax.all_gather(tokens, "col", axis=0, tiled=True)
    first = jnp.dot(gathered, gate_weight, preferred_element_type=jnp.float32)
    second = jnp.dot(gathered, up_weight, preferred_element_type=jnp.float32)
    joined = lax.psum_scatter(
        jnp.concatenate([first, second], axis=1).astype(jnp.bfloat16),
        "row",
        scatter_dimension=0,
        tiled=True,
    ).astype(jnp.float32)
    gate = joined[:, :width]
    up = joined[:, width:]
    sigma = jax.nn.sigmoid(gate)
    active = gate * sigma
    hidden = (active * up).astype(jnp.bfloat16)
    upstream = cotangent.astype(jnp.float32)
    grad_gate = (upstream * up * sigma * (1.0 + gate * (1.0 - sigma))).astype(jnp.bfloat16)
    grad_up = (upstream * active).astype(jnp.bfloat16)
    full_gate = lax.all_gather(grad_gate, "row", axis=0, tiled=True)
    sum_gate = weight_grad(gathered, full_gate, dep)
    full_up = lax.all_gather(grad_up, "row", axis=0, tiled=True)
    sum_up = weight_grad(gathered, full_up, dep)
    transposed = (((1,), (1,)), ((), ()))
    term = lax.dot_general(full_gate, gate_weight, transposed, preferred_element_type=jnp.float32)
    grad_tokens = lax.psum_scatter(
        (
            term
            + lax.dot_general(full_up, up_weight, transposed, preferred_element_type=jnp.float32)
        ).astype(jnp.bfloat16),
        "col",
        scatter_dimension=0,
        tiled=True,
    )
    return (hidden, grad_tokens, sum_gate, sum_up)


def solution(mesh):
    return jax.shard_map(
        on_device,
        mesh=mesh,
        in_specs=(
            P(("dep", "col"), "row"),
            P("row", "col"),
            P("row", "col"),
            P(("dep", "row"), "col"),
        ),
        out_specs=(
            P(("dep", "row"), "col"),
            P(("dep", "col"), "row"),
            P("row", ("col", "dep")),
            P("row", ("col", "dep")),
        ),
        check_vma=False,
    )
```

```python
import jax
import jax.numpy as jnp
from jax import lax
from jax.sharding import PartitionSpec as P


def halves(x, dep, half):
    own = lax.dynamic_slice_in_dim(x, dep * half, half, axis=1)
    other = lax.dynamic_slice_in_dim(x, (1 - dep) * half, half, axis=1)
    return own, other


def on_device(tokens, gate_weight, up_weight, cotangent):
    width = gate_weight.shape[1]
    half = width // 2
    dep = lax.axis_index("dep")
    gathered = lax.all_gather(tokens, "col", axis=0, tiled=True)
    first = jnp.dot(gathered, gate_weight, preferred_element_type=jnp.float32)
    second = jnp.dot(gathered, up_weight, preferred_element_type=jnp.float32)
    joined = lax.psum_scatter(
        jnp.concatenate([first, second], axis=1).astype(jnp.bfloat16),
        "row",
        scatter_dimension=0,
        tiled=True,
    ).astype(jnp.float32)
    gate = joined[:, :width]
    up = joined[:, width:]
    sigma = jax.nn.sigmoid(gate)
    active = gate * sigma
    hidden = (active * up).astype(jnp.bfloat16)
    upstream = cotangent.astype(jnp.float32)
    grad_gate = (upstream * up * sigma * (1.0 + gate * (1.0 - sigma))).astype(jnp.bfloat16)
    grad_up = (upstream * active).astype(jnp.bfloat16)

    gate_own, gate_other = halves(grad_gate, dep, half)
    up_own, up_other = halves(grad_up, dep, half)
    contract = (((0,), (0,)), ((), ()))
    transposed = (((1,), (1,)), ((), ()))

    full_other = lax.all_gather(
        jnp.concatenate([gate_other, up_other], axis=1), "row", axis=0, tiled=True
    )
    send = lax.dot_general(gathered, full_other, contract, preferred_element_type=jnp.float32)
    recv = lax.ppermute(send.astype(jnp.bfloat16), "dep", [(0, 1), (1, 0)])

    full_own = lax.all_gather(
        jnp.concatenate([gate_own, up_own], axis=1), "row", axis=0, tiled=True
    )
    mine = lax.dot_general(gathered, full_own, contract, preferred_element_type=jnp.float32)

    wg_own, wg_other = halves(gate_weight, dep, half)
    wu_own, wu_other = halves(up_weight, dep, half)
    term = lax.dot_general(
        full_other, jnp.concatenate([wg_other, wu_other], axis=1), transposed,
        preferred_element_type=jnp.float32,
    ) + lax.dot_general(
        full_own, jnp.concatenate([wg_own, wu_own], axis=1), transposed,
        preferred_element_type=jnp.float32,
    )
    grad_tokens = lax.psum_scatter(
        term.astype(jnp.bfloat16), "col", scatter_dimension=0, tiled=True
    )

    total = (mine.astype(jnp.bfloat16).astype(jnp.float32) + recv.astype(jnp.float32)).astype(
        jnp.bfloat16
    )
    return (hidden, grad_tokens, total[:, :half], total[:, half:])


def solution(mesh):
    return jax.shard_map(
        on_device,
        mesh=mesh,
        in_specs=(
            P(("dep", "col"), "row"),
            P("row", "col"),
            P("row", "col"),
            P(("dep", "row"), "col"),
        ),
        out_specs=(
            P(("dep", "row"), "col"),
            P(("dep", "col"), "row"),
            P("row", ("col", "dep")),
            P("row", ("col", "dep")),
        ),
        check_vma=False,
    )
```

```python
import jax
import jax.numpy as jnp
from jax import lax
from jax.sharding import PartitionSpec as P


def halves(x, dep, half):
    own = lax.dynamic_slice_in_dim(x, dep * half, half, axis=1)
    other = lax.dynamic_slice_in_dim(x, (1 - dep) * half, half, axis=1)
    return own, other


def on_device(tokens, gate_weight, up_weight, cotangent):
    width = gate_weight.shape[1]
    half = width // 2
    dep = lax.axis_index("dep")
    n_col = lax.axis_size("col")
    gathered = lax.all_to_all(
        jnp.tile(tokens, (n_col, 1)), "col", 0, 0, tiled=True
    )
    first = jnp.dot(gathered, gate_weight, preferred_element_type=jnp.float32)
    second = jnp.dot(gathered, up_weight, preferred_element_type=jnp.float32)
    joined = lax.psum_scatter(
        jnp.concatenate([first, second], axis=1).astype(jnp.bfloat16),
        "row",
        scatter_dimension=0,
        tiled=True,
    ).astype(jnp.float32)
    gate = joined[:, :width]
    up = joined[:, width:]
    sigma = jax.nn.sigmoid(gate)
    active = gate * sigma
    hidden = (active * up).astype(jnp.bfloat16)
    upstream = cotangent.astype(jnp.float32)
    grad_gate = (upstream * up * sigma * (1.0 + gate * (1.0 - sigma))).astype(jnp.bfloat16)
    grad_up = (upstream * active).astype(jnp.bfloat16)

    gate_own, gate_other = halves(grad_gate, dep, half)
    up_own, up_other = halves(grad_up, dep, half)
    contract = (((0,), (0,)), ((), ()))
    transposed = (((1,), (1,)), ((), ()))

    full_other = lax.all_gather(
        jnp.concatenate([gate_other, up_other], axis=1), "row", axis=0, tiled=True
    )
    send = lax.dot_general(gathered, full_other, contract, preferred_element_type=jnp.float32)
    recv = lax.ppermute(send.astype(jnp.bfloat16), "dep", [(0, 1), (1, 0)])

    full_own = lax.all_gather(
        jnp.concatenate([gate_own, up_own], axis=1), "row", axis=0, tiled=True
    )
    mine = lax.dot_general(gathered, full_own, contract, preferred_element_type=jnp.float32)

    wg_own, wg_other = halves(gate_weight, dep, half)
    wu_own, wu_other = halves(up_weight, dep, half)
    term = lax.dot_general(
        full_other, jnp.concatenate([wg_other, wu_other], axis=1), transposed,
        preferred_element_type=jnp.float32,
    ) + lax.dot_general(
        full_own, jnp.concatenate([wg_own, wu_own], axis=1), transposed,
        preferred_element_type=jnp.float32,
    )
    grad_tokens = lax.psum_scatter(
        term.astype(jnp.bfloat16), "col", scatter_dimension=0, tiled=True
    )

    total = (mine.astype(jnp.bfloat16).astype(jnp.float32) + recv.astype(jnp.float32)).astype(
        jnp.bfloat16
    )
    return (hidden, grad_tokens, total[:, :half], total[:, half:])


def solution(mesh):
    return jax.shard_map(
        on_device,
        mesh=mesh,
        in_specs=(
            P(("dep", "col"), "row"),
            P("row", "col"),
            P("row", "col"),
            P(("dep", "row"), "col"),
        ),
        out_specs=(
            P(("dep", "row"), "col"),
            P(("dep", "col"), "row"),
            P("row", ("col", "dep")),
            P("row", ("col", "dep")),
        ),
        check_vma=False,
    )
```

```python
import jax
import jax.numpy as jnp
from jax import lax
from jax.sharding import PartitionSpec as P


def halves(x, dep, half):
    own = lax.dynamic_slice_in_dim(x, dep * half, half, axis=1)
    other = lax.dynamic_slice_in_dim(x, (1 - dep) * half, half, axis=1)
    return own, other


def on_device(tokens, gate_weight, up_weight, cotangent):
    width = gate_weight.shape[1]
    half = width // 2
    dep = lax.axis_index("dep")
    n_col = lax.axis_size("col")
    gathered = lax.all_to_all(
        jnp.tile(tokens, (n_col, 1)), "col", 0, 0, tiled=True
    )
    def project(weight):
        part = jnp.dot(gathered, weight, preferred_element_type=jnp.float32)
        return lax.psum_scatter(
            part.astype(jnp.bfloat16), "row", scatter_dimension=0, tiled=True
        ).astype(jnp.float32)

    gate = project(gate_weight)
    up = project(up_weight)
    sigma = jax.nn.sigmoid(gate)
    active = gate * sigma
    hidden = (active * up).astype(jnp.bfloat16)
    upstream = cotangent.astype(jnp.float32)
    grad_gate = (upstream * up * sigma * (1.0 + gate * (1.0 - sigma))).astype(jnp.bfloat16)
    grad_up = (upstream * active).astype(jnp.bfloat16)

    gate_own, gate_other = halves(grad_gate, dep, half)
    up_own, up_other = halves(grad_up, dep, half)
    contract = (((0,), (0,)), ((), ()))
    transposed = (((1,), (1,)), ((), ()))

    full_other = lax.all_gather(
        jnp.concatenate([gate_other, up_other], axis=1), "row", axis=0, tiled=True
    )
    send = lax.dot_general(gathered, full_other, contract, preferred_element_type=jnp.float32)
    recv = lax.ppermute(send.astype(jnp.bfloat16), "dep", [(0, 1), (1, 0)])

    full_own = lax.all_gather(
        jnp.concatenate([gate_own, up_own], axis=1), "row", axis=0, tiled=True
    )
    mine = lax.dot_general(gathered, full_own, contract, preferred_element_type=jnp.float32)

    wg_own, wg_other = halves(gate_weight, dep, half)
    wu_own, wu_other = halves(up_weight, dep, half)
    term = lax.dot_general(
        full_other, jnp.concatenate([wg_other, wu_other], axis=1), transposed,
        preferred_element_type=jnp.float32,
    ) + lax.dot_general(
        full_own, jnp.concatenate([wg_own, wu_own], axis=1), transposed,
        preferred_element_type=jnp.float32,
    )
    grad_tokens = lax.psum_scatter(
        term.astype(jnp.bfloat16), "col", scatter_dimension=0, tiled=True
    )

    total = (mine.astype(jnp.bfloat16).astype(jnp.float32) + recv.astype(jnp.float32)).astype(
        jnp.bfloat16
    )
    return (hidden, grad_tokens, total[:, :half], total[:, half:])


def solution(mesh):
    return jax.shard_map(
        on_device,
        mesh=mesh,
        in_specs=(
            P(("dep", "col"), "row"),
            P("row", "col"),
            P("row", "col"),
            P(("dep", "row"), "col"),
        ),
        out_specs=(
            P(("dep", "row"), "col"),
            P(("dep", "col"), "row"),
            P("row", ("col", "dep")),
            P("row", ("col", "dep")),
        ),
        check_vma=False,
    )
```

```python
import jax
import jax.numpy as jnp
from jax import lax
from jax.sharding import PartitionSpec as P


def halves(x, dep, half):
    own = lax.dynamic_slice_in_dim(x, dep * half, half, axis=1)
    other = lax.dynamic_slice_in_dim(x, (1 - dep) * half, half, axis=1)
    return own, other


def on_device(tokens, gate_weight, up_weight, cotangent):
    width = gate_weight.shape[1]
    half = width // 2
    dep = lax.axis_index("dep")
    n_col = lax.axis_size("col")
    contract = (((0,), (0,)), ((), ()))
    transposed = (((1,), (1,)), ((), ()))
    pair = [(0, 1), (1, 0)]

    def gather_col(block):
        return lax.all_to_all(jnp.tile(block, (n_col, 1)), "col", 0, 0, tiled=True)

    partner_tokens = lax.ppermute(tokens, "dep", pair)
    gathered = gather_col(tokens)
    first = jnp.dot(gathered, gate_weight, preferred_element_type=jnp.float32)
    second = jnp.dot(gathered, up_weight, preferred_element_type=jnp.float32)
    joined = lax.psum_scatter(
        jnp.concatenate([first, second], axis=1).astype(jnp.bfloat16),
        "row",
        scatter_dimension=0,
        tiled=True,
    )
    gathered_partner = gather_col(partner_tokens)
    joined, gathered_partner = lax.optimization_barrier((joined, gathered_partner))
    joined = joined.astype(jnp.float32)
    gate = joined[:, :width]
    up = joined[:, width:]
    sigma = jax.nn.sigmoid(gate)
    active = gate * sigma
    hidden = (active * up).astype(jnp.bfloat16)
    upstream = cotangent.astype(jnp.float32)
    grad_gate = (upstream * up * sigma * (1.0 + gate * (1.0 - sigma))).astype(jnp.bfloat16)
    grad_up = (upstream * active).astype(jnp.bfloat16)

    gate_own, gate_other = halves(grad_gate, dep, half)
    up_own, up_other = halves(grad_up, dep, half)
    partner_grads = lax.ppermute(
        jnp.concatenate([gate_other, up_other], axis=1), "dep", pair
    )
    full = lax.all_gather(
        jnp.concatenate([grad_gate, grad_up, partner_grads], axis=1),
        "row", axis=0, tiled=True,
    )
    full_gate = full[:, :width]
    full_up = full[:, width:2 * width]
    full_partner = full[:, 2 * width:]

    term = lax.dot_general(full_gate, gate_weight, transposed, preferred_element_type=jnp.float32)
    term = term + lax.dot_general(full_up, up_weight, transposed, preferred_element_type=jnp.float32)
    grad_tokens = lax.psum_scatter(
        term.astype(jnp.bfloat16), "col", scatter_dimension=0, tiled=True
    )

    own_cols = jnp.concatenate(
        [lax.dynamic_slice_in_dim(full_gate, dep * half, half, axis=1),
         lax.dynamic_slice_in_dim(full_up, dep * half, half, axis=1)],
        axis=1,
    )
    mine = lax.dot_general(gathered, own_cols, contract, preferred_element_type=jnp.float32)
    theirs = lax.dot_general(
        gathered_partner, full_partner, contract, preferred_element_type=jnp.float32
    )
    total = (
        mine.astype(jnp.bfloat16).astype(jnp.float32)
        + theirs.astype(jnp.bfloat16).astype(jnp.float32)
    ).astype(jnp.bfloat16)
    return (hidden, grad_tokens, total[:, :half], total[:, half:])


def solution(mesh):
    return jax.shard_map(
        on_device,
        mesh=mesh,
        in_specs=(
            P(("dep", "col"), "row"),
            P("row", "col"),
            P("row", "col"),
            P(("dep", "row"), "col"),
        ),
        out_specs=(
            P(("dep", "row"), "col"),
            P(("dep", "col"), "row"),
            P("row", ("col", "dep")),
            P("row", ("col", "dep")),
        ),
        check_vma=False,
    )
```

```python
import jax
import jax.numpy as jnp
from jax import lax
from jax.sharding import PartitionSpec as P


def halves(x, dep, half):
    own = lax.dynamic_slice_in_dim(x, dep * half, half, axis=1)
    other = lax.dynamic_slice_in_dim(x, (1 - dep) * half, half, axis=1)
    return own, other


def on_device(tokens, gate_weight, up_weight, cotangent):
    width = gate_weight.shape[1]
    half = width // 2
    dep = lax.axis_index("dep")
    n_col = lax.axis_size("col")
    contract = (((0,), (0,)), ((), ()))
    transposed = (((1,), (1,)), ((), ()))
    pair = [(0, 1), (1, 0)]

    def gather_col(block):
        return lax.all_to_all(jnp.tile(block, (n_col, 1)), "col", 0, 0, tiled=True)

    partner_tokens = lax.ppermute(tokens, "dep", pair)
    gathered = gather_col(tokens)
    first = jnp.dot(gathered, gate_weight, preferred_element_type=jnp.float32)
    second = jnp.dot(gathered, up_weight, preferred_element_type=jnp.float32)
    joined = lax.psum_scatter(
        jnp.concatenate([first, second], axis=1).astype(jnp.bfloat16),
        "row",
        scatter_dimension=0,
        tiled=True,
    )
    gathered_partner = gather_col(partner_tokens)
    joined, gathered_partner = lax.optimization_barrier((joined, gathered_partner))
    joined = joined.astype(jnp.float32)
    gate = joined[:, :width]
    up = joined[:, width:]
    sigma = jax.nn.sigmoid(gate)
    active = gate * sigma
    hidden = (active * up).astype(jnp.bfloat16)
    upstream = cotangent.astype(jnp.float32)
    grad_gate = (upstream * up * sigma * (1.0 + gate * (1.0 - sigma))).astype(jnp.bfloat16)
    grad_up = (upstream * active).astype(jnp.bfloat16)

    gate_own, gate_other = halves(grad_gate, dep, half)
    up_own, up_other = halves(grad_up, dep, half)
    partner_grads = lax.ppermute(
        jnp.concatenate([gate_other, up_other], axis=1), "dep", pair
    )
    full = lax.all_gather(
        jnp.concatenate([grad_gate, grad_up, partner_grads], axis=1),
        "row", axis=0, tiled=True,
    )
    full_gate = full[:, :width]
    full_up = full[:, width:2 * width]
    full_partner = full[:, 2 * width:]

    term = lax.dot_general(full_gate, gate_weight, transposed, preferred_element_type=jnp.float32)
    term = term + lax.dot_general(full_up, up_weight, transposed, preferred_element_type=jnp.float32)
    parts = lax.all_to_all(
        term.astype(jnp.bfloat16).reshape(n_col, -1, term.shape[1]), "col", 0, 0, tiled=True
    )
    grad_tokens = parts.astype(jnp.float32).sum(axis=0).astype(jnp.bfloat16)

    own_cols = jnp.concatenate(
        [lax.dynamic_slice_in_dim(full_gate, dep * half, half, axis=1),
         lax.dynamic_slice_in_dim(full_up, dep * half, half, axis=1)],
        axis=1,
    )
    mine = lax.dot_general(gathered, own_cols, contract, preferred_element_type=jnp.float32)
    theirs = lax.dot_general(
        gathered_partner, full_partner, contract, preferred_element_type=jnp.float32
    )
    total = (
        mine.astype(jnp.bfloat16).astype(jnp.float32)
        + theirs.astype(jnp.bfloat16).astype(jnp.float32)
    ).astype(jnp.bfloat16)
    return (hidden, grad_tokens, total[:, :half], total[:, half:])


def solution(mesh):
    return jax.shard_map(
        on_device,
        mesh=mesh,
        in_specs=(
            P(("dep", "col"), "row"),
            P("row", "col"),
            P("row", "col"),
            P(("dep", "row"), "col"),
        ),
        out_specs=(
            P(("dep", "row"), "col"),
            P(("dep", "col"), "row"),
            P("row", ("col", "dep")),
            P("row", ("col", "dep")),
        ),
        check_vma=False,
    )
```

```python
import jax
import jax.numpy as jnp
from jax import lax
from jax.sharding import PartitionSpec as P


def halves(x, dep, half):
    own = lax.dynamic_slice_in_dim(x, dep * half, half, axis=1)
    other = lax.dynamic_slice_in_dim(x, (1 - dep) * half, half, axis=1)
    return own, other


def on_device(tokens, gate_weight, up_weight, cotangent):
    width = gate_weight.shape[1]
    half = width // 2
    dep = lax.axis_index("dep")
    n_col = lax.axis_size("col")
    contract = (((0,), (0,)), ((), ()))
    transposed = (((1,), (1,)), ((), ()))
    pair = [(0, 1), (1, 0)]

    def gather_col(block):
        return lax.all_to_all(jnp.tile(block, (n_col, 1)), "col", 0, 0, tiled=True)

    partner_tokens = lax.ppermute(tokens, "dep", pair)
    gathered = gather_col(tokens)
    first = jnp.dot(gathered, gate_weight, preferred_element_type=jnp.float32)
    second = jnp.dot(gathered, up_weight, preferred_element_type=jnp.float32)
    joined = lax.psum_scatter(
        jnp.concatenate([first, second], axis=1).astype(jnp.bfloat16),
        "row",
        scatter_dimension=0,
        tiled=True,
    )
    gathered_partner = gather_col(partner_tokens)
    joined, gathered_partner = lax.optimization_barrier((joined, gathered_partner))
    joined = joined.astype(jnp.float32)
    gate = joined[:, :width]
    up = joined[:, width:]
    sigma = jax.nn.sigmoid(gate)
    active = gate * sigma
    hidden = (active * up).astype(jnp.bfloat16)
    upstream = cotangent.astype(jnp.float32)
    grad_gate = (upstream * up * sigma * (1.0 + gate * (1.0 - sigma))).astype(jnp.bfloat16)
    grad_up = (upstream * active).astype(jnp.bfloat16)

    gate_own, gate_other = halves(grad_gate, dep, half)
    up_own, up_other = halves(grad_up, dep, half)
    partner_grads = lax.ppermute(
        jnp.concatenate([gate_other, up_other], axis=1), "dep", pair
    )
    full = lax.all_gather(
        jnp.concatenate([grad_gate, grad_up, partner_grads], axis=1),
        "row", axis=0, tiled=True,
    )
    full_gate = full[:, :width]
    full_up = full[:, width:2 * width]
    full_partner = full[:, 2 * width:]

    term = lax.dot_general(full_gate, gate_weight, transposed, preferred_element_type=jnp.float32)
    term = term + lax.dot_general(full_up, up_weight, transposed, preferred_element_type=jnp.float32)
    term = term.astype(jnp.bfloat16).reshape(n_col, -1, term.shape[1])

    own_cols = jnp.concatenate(
        [lax.dynamic_slice_in_dim(full_gate, dep * half, half, axis=1),
         lax.dynamic_slice_in_dim(full_up, dep * half, half, axis=1)],
        axis=1,
    )
    own_cols, full_partner, term = lax.optimization_barrier((own_cols, full_partner, term))
    parts = lax.all_to_all(term, "col", 0, 0, tiled=True)
    grad_tokens = parts.astype(jnp.float32).sum(axis=0).astype(jnp.bfloat16)

    def weight_part(grads, rows):
        return lax.dot_general(rows, grads, contract, preferred_element_type=jnp.float32)

    mine = weight_part(own_cols, gathered)
    theirs = weight_part(full_partner, gathered_partner)
    total = (
        mine.astype(jnp.bfloat16).astype(jnp.float32)
        + theirs.astype(jnp.bfloat16).astype(jnp.float32)
    ).astype(jnp.bfloat16)
    return (hidden, grad_tokens, total[:, :half], total[:, half:])


def solution(mesh):
    return jax.shard_map(
        on_device,
        mesh=mesh,
        in_specs=(
            P(("dep", "col"), "row"),
            P("row", "col"),
            P("row", "col"),
            P(("dep", "row"), "col"),
        ),
        out_specs=(
            P(("dep", "row"), "col"),
            P(("dep", "col"), "row"),
            P("row", ("col", "dep")),
            P("row", ("col", "dep")),
        ),
        check_vma=False,
    )
```

```python
import jax
import jax.numpy as jnp
from jax import lax
from jax.sharding import PartitionSpec as P


def halves(x, dep, half):
    own = lax.dynamic_slice_in_dim(x, dep * half, half, axis=1)
    other = lax.dynamic_slice_in_dim(x, (1 - dep) * half, half, axis=1)
    return own, other


def on_device(tokens, gate_weight, up_weight, cotangent):
    width = gate_weight.shape[1]
    half = width // 2
    dep = lax.axis_index("dep")
    n_col = lax.axis_size("col")
    contract = (((0,), (0,)), ((), ()))
    transposed = (((1,), (1,)), ((), ()))
    pair = [(0, 1), (1, 0)]

    def gather_col(block):
        return lax.all_to_all(jnp.tile(block, (n_col, 1)), "col", 0, 0, tiled=True)

    partner_tokens = lax.ppermute(tokens, "dep", pair)
    gathered = gather_col(tokens)
    first = jnp.dot(gathered, gate_weight, preferred_element_type=jnp.float32)
    second = jnp.dot(gathered, up_weight, preferred_element_type=jnp.float32)
    joined = lax.psum_scatter(
        jnp.concatenate([first, second], axis=1).astype(jnp.bfloat16),
        "row",
        scatter_dimension=0,
        tiled=True,
    )
    gathered_partner = gather_col(partner_tokens)
    joined, gathered_partner = lax.optimization_barrier((joined, gathered_partner))
    joined = joined.astype(jnp.float32)
    gate = joined[:, :width]
    up = joined[:, width:]
    sigma = jax.nn.sigmoid(gate)
    active = gate * sigma
    hidden = (active * up).astype(jnp.bfloat16)
    upstream = cotangent.astype(jnp.float32)
    grad_gate = (upstream * up * sigma * (1.0 + gate * (1.0 - sigma))).astype(jnp.bfloat16)
    grad_up = (upstream * active).astype(jnp.bfloat16)

    gate_own, gate_other = halves(grad_gate, dep, half)
    up_own, up_other = halves(grad_up, dep, half)
    partner_grads = lax.ppermute(
        jnp.concatenate([gate_other, up_other], axis=1), "dep", pair
    )
    full = lax.all_gather(
        jnp.stack([grad_gate, grad_up, partner_grads]), "row", axis=1, tiled=True
    )
    full_gate, full_up, full_partner = full[0], full[1], full[2]

    term = lax.dot_general(full_gate, gate_weight, transposed, preferred_element_type=jnp.float32)
    term = term + lax.dot_general(full_up, up_weight, transposed, preferred_element_type=jnp.float32)
    term = term.astype(jnp.bfloat16).reshape(n_col, -1, term.shape[1])

    own_cols = jnp.concatenate(
        [lax.dynamic_slice_in_dim(full_gate, dep * half, half, axis=1),
         lax.dynamic_slice_in_dim(full_up, dep * half, half, axis=1)],
        axis=1,
    )
    own_cols, full_partner, term = lax.optimization_barrier((own_cols, full_partner, term))
    parts = lax.all_to_all(term, "col", 0, 0, tiled=True)
    grad_tokens = parts.astype(jnp.float32).sum(axis=0).astype(jnp.bfloat16)

    def weight_part(grads, rows):
        return lax.dot_general(rows, grads, contract, preferred_element_type=jnp.float32)

    mine = weight_part(own_cols, gathered)
    theirs = weight_part(full_partner, gathered_partner)
    total = (
        mine.astype(jnp.bfloat16).astype(jnp.float32)
        + theirs.astype(jnp.bfloat16).astype(jnp.float32)
    ).astype(jnp.bfloat16)
    return (hidden, grad_tokens, total[:, :half], total[:, half:])


def solution(mesh):
    return jax.shard_map(
        on_device,
        mesh=mesh,
        in_specs=(
            P(("dep", "col"), "row"),
            P("row", "col"),
            P("row", "col"),
            P(("dep", "row"), "col"),
        ),
        out_specs=(
            P(("dep", "row"), "col"),
            P(("dep", "col"), "row"),
            P("row", ("col", "dep")),
            P("row", ("col", "dep")),
        ),
        check_vma=False,
    )
```

```python
import jax
import jax.numpy as jnp
from jax import lax
from jax.sharding import PartitionSpec as P


def halves(x, dep, half):
    own = lax.dynamic_slice_in_dim(x, dep * half, half, axis=1)
    other = lax.dynamic_slice_in_dim(x, (1 - dep) * half, half, axis=1)
    return own, other


def on_device(tokens, gate_weight, up_weight, cotangent):
    width = gate_weight.shape[1]
    half = width // 2
    dep = lax.axis_index("dep")
    n_col = lax.axis_size("col")
    contract = (((0,), (0,)), ((), ()))
    transposed = (((1,), (1,)), ((), ()))
    pair = [(0, 1), (1, 0)]

    def gather_col(block):
        return lax.all_to_all(jnp.tile(block, (n_col, 1)), "col", 0, 0, tiled=True)

    partner_tokens = lax.ppermute(tokens, "dep", pair)
    gathered = gather_col(tokens)
    first = jnp.dot(gathered, gate_weight, preferred_element_type=jnp.float32)
    second = jnp.dot(gathered, up_weight, preferred_element_type=jnp.float32)
    joined = lax.psum_scatter(
        jnp.concatenate([first, second], axis=1).astype(jnp.bfloat16),
        "row",
        scatter_dimension=0,
        tiled=True,
    )
    gathered_partner = gather_col(partner_tokens)
    joined, gathered_partner = lax.optimization_barrier((joined, gathered_partner))
    joined = joined.astype(jnp.float32)
    gate = joined[:, :width]
    up = joined[:, width:]
    sigma = jax.nn.sigmoid(gate)
    active = gate * sigma
    hidden = (active * up).astype(jnp.bfloat16)
    upstream = cotangent.astype(jnp.float32)
    grad_gate = (upstream * up * sigma * (1.0 + gate * (1.0 - sigma))).astype(jnp.bfloat16)
    grad_up = (upstream * active).astype(jnp.bfloat16)

    gate_own, gate_other = halves(grad_gate, dep, half)
    up_own, up_other = halves(grad_up, dep, half)
    partner_gate, partner_up = jnp.split(
        lax.ppermute(jnp.concatenate([gate_other, up_other], axis=1), "dep", pair), 2, axis=1
    )
    full = lax.all_gather(
        jnp.stack([gate_own, up_own, gate_other, up_other, partner_gate, partner_up]),
        "row", axis=1, tiled=True,
    )

    wg_own, wg_other = halves(gate_weight, dep, half)
    wu_own, wu_other = halves(up_weight, dep, half)
    term = lax.dot_general(full[0], wg_own, transposed, preferred_element_type=jnp.float32)
    term = term + lax.dot_general(full[2], wg_other, transposed, preferred_element_type=jnp.float32)
    term = term + lax.dot_general(full[1], wu_own, transposed, preferred_element_type=jnp.float32)
    term = term + lax.dot_general(full[3], wu_other, transposed, preferred_element_type=jnp.float32)
    term = term.astype(jnp.bfloat16).reshape(n_col, -1, term.shape[1])
    term, gathered, gathered_partner = lax.optimization_barrier((term, gathered, gathered_partner))
    parts = lax.all_to_all(term, "col", 0, 0, tiled=True)
    grad_tokens = parts.astype(jnp.float32).sum(axis=0).astype(jnp.bfloat16)

    def weight_grad(own, partner):
        mine = lax.dot_general(gathered, own, contract, preferred_element_type=jnp.float32)
        theirs = lax.dot_general(
            gathered_partner, partner, contract, preferred_element_type=jnp.float32
        )
        return (
            mine.astype(jnp.bfloat16).astype(jnp.float32)
            + theirs.astype(jnp.bfloat16).astype(jnp.float32)
        ).astype(jnp.bfloat16)

    sum_gate = weight_grad(full[0], full[4])
    sum_up = weight_grad(full[1], full[5])
    return (hidden, grad_tokens, sum_gate, sum_up)


def solution(mesh):
    return jax.shard_map(
        on_device,
        mesh=mesh,
        in_specs=(
            P(("dep", "col"), "row"),
            P("row", "col"),
            P("row", "col"),
            P(("dep", "row"), "col"),
        ),
        out_specs=(
            P(("dep", "row"), "col"),
            P(("dep", "col"), "row"),
            P("row", ("col", "dep")),
            P("row", ("col", "dep")),
        ),
        check_vma=False,
    )
```

```python
import jax
import jax.numpy as jnp
from jax import lax
from jax.sharding import PartitionSpec as P


def halves(x, dep, half):
    own = lax.dynamic_slice_in_dim(x, dep * half, half, axis=1)
    other = lax.dynamic_slice_in_dim(x, (1 - dep) * half, half, axis=1)
    return own, other


def on_device(tokens, gate_weight, up_weight, cotangent):
    width = gate_weight.shape[1]
    half = width // 2
    dep = lax.axis_index("dep")
    n_col = lax.axis_size("col")
    contract = (((0,), (0,)), ((), ()))
    transposed = (((1,), (1,)), ((), ()))
    pair = [(0, 1), (1, 0)]

    def gather_col(block):
        return lax.all_to_all(jnp.tile(block, (n_col, 1)), "col", 0, 0, tiled=True)

    partner_tokens = lax.ppermute(tokens, "dep", pair)
    feat = tokens.shape[1] // 2
    lower = gather_col(tokens[:, :feat])
    first = jnp.dot(lower, gate_weight[:feat], preferred_element_type=jnp.float32)
    second = jnp.dot(lower, up_weight[:feat], preferred_element_type=jnp.float32)
    upper = gather_col(tokens[:, feat:])
    first = first + jnp.dot(upper, gate_weight[feat:], preferred_element_type=jnp.float32)
    second = second + jnp.dot(upper, up_weight[feat:], preferred_element_type=jnp.float32)
    gathered = jnp.concatenate([lower, upper], axis=1)
    joined = lax.psum_scatter(
        jnp.concatenate([first, second], axis=1).astype(jnp.bfloat16),
        "row",
        scatter_dimension=0,
        tiled=True,
    )
    gathered_partner = gather_col(partner_tokens)
    joined, gathered_partner = lax.optimization_barrier((joined, gathered_partner))
    joined = joined.astype(jnp.float32)
    gate = joined[:, :width]
    up = joined[:, width:]
    sigma = jax.nn.sigmoid(gate)
    active = gate * sigma
    hidden = (active * up).astype(jnp.bfloat16)
    upstream = cotangent.astype(jnp.float32)
    grad_gate = (upstream * up * sigma * (1.0 + gate * (1.0 - sigma))).astype(jnp.bfloat16)
    grad_up = (upstream * active).astype(jnp.bfloat16)

    gate_own, gate_other = halves(grad_gate, dep, half)
    up_own, up_other = halves(grad_up, dep, half)
    partner_gate, partner_up = jnp.split(
        lax.ppermute(jnp.concatenate([gate_other, up_other], axis=1), "dep", pair), 2, axis=1
    )
    full = lax.all_gather(
        jnp.stack([gate_own, up_own, gate_other, up_other, partner_gate, partner_up]),
        "row", axis=1, tiled=True,
    )

    wg_own, wg_other = halves(gate_weight, dep, half)
    wu_own, wu_other = halves(up_weight, dep, half)
    def grad_part(lo, hi):
        term = lax.dot_general(full[0], wg_own[lo:hi], transposed, preferred_element_type=jnp.float32)
        term = term + lax.dot_general(
            full[2], wg_other[lo:hi], transposed, preferred_element_type=jnp.float32
        )
        term = term + lax.dot_general(
            full[1], wu_own[lo:hi], transposed, preferred_element_type=jnp.float32
        )
        term = term + lax.dot_general(
            full[3], wu_other[lo:hi], transposed, preferred_element_type=jnp.float32
        )
        return term.astype(jnp.bfloat16).reshape(n_col, -1, hi - lo)

    def reduce_part(term):
        parts = lax.all_to_all(term, "col", 0, 0, tiled=True)
        return parts.astype(jnp.float32).sum(axis=0).astype(jnp.bfloat16)

    rows = gate_weight.shape[0]
    low_sum = reduce_part(grad_part(0, rows // 2))
    high = grad_part(rows // 2, rows)
    high, gathered, gathered_partner = lax.optimization_barrier((high, gathered, gathered_partner))
    grad_tokens = jnp.concatenate([low_sum, reduce_part(high)], axis=1)

    def weight_grad(own, partner):
        mine = lax.dot_general(gathered, own, contract, preferred_element_type=jnp.float32)
        theirs = lax.dot_general(
            gathered_partner, partner, contract, preferred_element_type=jnp.float32
        )
        return (
            mine.astype(jnp.bfloat16).astype(jnp.float32)
            + theirs.astype(jnp.bfloat16).astype(jnp.float32)
        ).astype(jnp.bfloat16)

    sum_gate = weight_grad(full[0], full[4])
    sum_up = weight_grad(full[1], full[5])
    return (hidden, grad_tokens, sum_gate, sum_up)


def solution(mesh):
    return jax.shard_map(
        on_device,
        mesh=mesh,
        in_specs=(
            P(("dep", "col"), "row"),
            P("row", "col"),
            P("row", "col"),
            P(("dep", "row"), "col"),
        ),
        out_specs=(
            P(("dep", "row"), "col"),
            P(("dep", "col"), "row"),
            P("row", ("col", "dep")),
            P("row", ("col", "dep")),
        ),
        check_vma=False,
    )
```

```python
import jax
import jax.numpy as jnp
from jax import lax
from jax.sharding import PartitionSpec as P


def halves(x, dep, half):
    own = lax.dynamic_slice_in_dim(x, dep * half, half, axis=1)
    other = lax.dynamic_slice_in_dim(x, (1 - dep) * half, half, axis=1)
    return own, other


def on_device(tokens, gate_weight, up_weight, cotangent):
    width = gate_weight.shape[1]
    half = width // 2
    dep = lax.axis_index("dep")
    n_col = lax.axis_size("col")
    contract = (((0,), (0,)), ((), ()))
    transposed = (((1,), (1,)), ((), ()))
    pair = [(0, 1), (1, 0)]

    def gather_col(block):
        return lax.all_to_all(jnp.tile(block, (n_col, 1)), "col", 0, 0, tiled=True)

    partner_tokens = lax.ppermute(tokens, "dep", pair)
    gathered = gather_col(tokens)
    first = jnp.dot(gathered, gate_weight, preferred_element_type=jnp.float32)
    second = jnp.dot(gathered, up_weight, preferred_element_type=jnp.float32)
    joined = lax.psum_scatter(
        jnp.concatenate([first, second], axis=1).astype(jnp.bfloat16),
        "row",
        scatter_dimension=0,
        tiled=True,
    )
    gathered_partner = gather_col(partner_tokens)
    joined, gathered_partner = lax.optimization_barrier((joined, gathered_partner))
    joined = joined.astype(jnp.float32)
    gate = joined[:, :width]
    up = joined[:, width:]
    sigma = jax.nn.sigmoid(gate)
    active = gate * sigma
    hidden = (active * up).astype(jnp.bfloat16)
    upstream = cotangent.astype(jnp.float32)
    grad_gate = (upstream * up * sigma * (1.0 + gate * (1.0 - sigma))).astype(jnp.bfloat16)
    grad_up = (upstream * active).astype(jnp.bfloat16)

    gate_own, gate_other = halves(grad_gate, dep, half)
    up_own, up_other = halves(grad_up, dep, half)
    full = lax.all_gather(
        jnp.stack([gate_own, up_own, gate_other, up_other]), "row", axis=1, tiled=True
    )
    n_row = lax.axis_size("row")
    partner = lax.ppermute(jnp.stack([gate_other, up_other]), "dep", pair)
    partner = lax.all_to_all(
        jnp.broadcast_to(partner[None], (n_row,) + partner.shape), "row", 0, 0, tiled=True
    )
    partner_gate = partner[:, 0].reshape(-1, half)
    partner_up = partner[:, 1].reshape(-1, half)

    wg_own, wg_other = halves(gate_weight, dep, half)
    wu_own, wu_other = halves(up_weight, dep, half)
    term = lax.dot_general(full[0], wg_own, transposed, preferred_element_type=jnp.float32)
    term = term + lax.dot_general(full[2], wg_other, transposed, preferred_element_type=jnp.float32)
    term = term + lax.dot_general(full[1], wu_own, transposed, preferred_element_type=jnp.float32)
    term = term + lax.dot_general(full[3], wu_other, transposed, preferred_element_type=jnp.float32)
    term = term.astype(jnp.bfloat16).reshape(n_col, -1, term.shape[1])
    term, gathered, gathered_partner = lax.optimization_barrier((term, gathered, gathered_partner))
    parts = lax.all_to_all(term, "col", 0, 0, tiled=True)
    grad_tokens = parts.astype(jnp.float32).sum(axis=0).astype(jnp.bfloat16)

    def weight_grad(own, partner):
        mine = lax.dot_general(gathered, own, contract, preferred_element_type=jnp.float32)
        theirs = lax.dot_general(
            gathered_partner, partner, contract, preferred_element_type=jnp.float32
        )
        return (
            mine.astype(jnp.bfloat16).astype(jnp.float32)
            + theirs.astype(jnp.bfloat16).astype(jnp.float32)
        ).astype(jnp.bfloat16)

    sum_gate = weight_grad(full[0], partner_gate)
    sum_up = weight_grad(full[1], partner_up)
    return (hidden, grad_tokens, sum_gate, sum_up)


def solution(mesh):
    return jax.shard_map(
        on_device,
        mesh=mesh,
        in_specs=(
            P(("dep", "col"), "row"),
            P("row", "col"),
            P("row", "col"),
            P(("dep", "row"), "col"),
        ),
        out_specs=(
            P(("dep", "row"), "col"),
            P(("dep", "col"), "row"),
            P("row", ("col", "dep")),
            P("row", ("col", "dep")),
        ),
        check_vma=False,
    )
```

```python
import jax
import jax.numpy as jnp
from jax import lax
from jax.sharding import PartitionSpec as P


def halves(x, dep, half):
    own = lax.dynamic_slice_in_dim(x, dep * half, half, axis=1)
    other = lax.dynamic_slice_in_dim(x, (1 - dep) * half, half, axis=1)
    return own, other


def on_device(tokens, gate_weight, up_weight, cotangent):
    width = gate_weight.shape[1]
    half = width // 2
    dep = lax.axis_index("dep")
    n_col = lax.axis_size("col")
    contract = (((0,), (0,)), ((), ()))
    transposed = (((1,), (1,)), ((), ()))
    pair = [(0, 1), (1, 0)]

    def gather_col(block):
        return lax.all_to_all(jnp.tile(block, (n_col, 1)), "col", 0, 0, tiled=True)

    partner_tokens = lax.ppermute(tokens, "dep", pair)
    gathered = gather_col(tokens)
    first = jnp.dot(gathered, gate_weight, preferred_element_type=jnp.float32)
    second = jnp.dot(gathered, up_weight, preferred_element_type=jnp.float32)
    joined = lax.psum_scatter(
        jnp.concatenate([first, second], axis=1).astype(jnp.bfloat16),
        "row",
        scatter_dimension=0,
        tiled=True,
    )
    gathered_partner = gather_col(partner_tokens)
    joined, gathered_partner = lax.optimization_barrier((joined, gathered_partner))
    joined = joined.astype(jnp.float32)
    gate = joined[:, :width]
    up = joined[:, width:]
    sigma = jax.nn.sigmoid(gate)
    active = gate * sigma
    hidden = (active * up).astype(jnp.bfloat16)
    upstream = cotangent.astype(jnp.float32)
    grad_gate = (upstream * up * sigma * (1.0 + gate * (1.0 - sigma))).astype(jnp.bfloat16)
    grad_up = (upstream * active).astype(jnp.bfloat16)

    gate_own, gate_other = halves(grad_gate, dep, half)
    up_own, up_other = halves(grad_up, dep, half)
    partner_gate, partner_up = jnp.split(
        lax.ppermute(jnp.concatenate([gate_other, up_other], axis=1), "dep", pair), 2, axis=1
    )
    full = lax.all_gather(
        jnp.stack([gate_own, up_own, gate_other, up_other, partner_gate, partner_up]),
        "row", axis=1, tiled=True,
    )

    wg_own, wg_other = halves(gate_weight, dep, half)
    wu_own, wu_other = halves(up_weight, dep, half)
    term = lax.dot_general(full[0], wg_own, transposed, preferred_element_type=jnp.float32)
    term = term + lax.dot_general(full[2], wg_other, transposed, preferred_element_type=jnp.float32)
    term = term + lax.dot_general(full[1], wu_own, transposed, preferred_element_type=jnp.float32)
    term = term + lax.dot_general(full[3], wu_other, transposed, preferred_element_type=jnp.float32)
    term = term.astype(jnp.bfloat16).reshape(n_col, -1, term.shape[1])
    term, gathered, gathered_partner = lax.optimization_barrier((term, gathered, gathered_partner))
    col = lax.axis_index("col")
    summed = lax.dynamic_index_in_dim(term, col, 0, keepdims=False).astype(jnp.float32)
    for shift in range(1, n_col):
        block = lax.dynamic_index_in_dim(term, (col + shift) % n_col, 0, keepdims=False)
        moved = lax.ppermute(block, "col", [(i, (i + shift) % n_col) for i in range(n_col)])
        summed = summed + moved.astype(jnp.float32)
    grad_tokens = summed.astype(jnp.bfloat16)

    def weight_grad(own, partner):
        mine = lax.dot_general(gathered, own, contract, preferred_element_type=jnp.float32)
        theirs = lax.dot_general(
            gathered_partner, partner, contract, preferred_element_type=jnp.float32
        )
        return (
            mine.astype(jnp.bfloat16).astype(jnp.float32)
            + theirs.astype(jnp.bfloat16).astype(jnp.float32)
        ).astype(jnp.bfloat16)

    sum_gate = weight_grad(full[0], full[4])
    sum_up = weight_grad(full[1], full[5])
    return (hidden, grad_tokens, sum_gate, sum_up)


def solution(mesh):
    return jax.shard_map(
        on_device,
        mesh=mesh,
        in_specs=(
            P(("dep", "col"), "row"),
            P("row", "col"),
            P("row", "col"),
            P(("dep", "row"), "col"),
        ),
        out_specs=(
            P(("dep", "row"), "col"),
            P(("dep", "col"), "row"),
            P("row", ("col", "dep")),
            P("row", ("col", "dep")),
        ),
        check_vma=False,
    )
```

```python
import jax
import jax.numpy as jnp
from jax import lax
from jax.sharding import PartitionSpec as P


def halves(x, dep, half):
    own = lax.dynamic_slice_in_dim(x, dep * half, half, axis=1)
    other = lax.dynamic_slice_in_dim(x, (1 - dep) * half, half, axis=1)
    return own, other


def on_device(tokens, gate_weight, up_weight, cotangent):
    width = gate_weight.shape[1]
    half = width // 2
    dep = lax.axis_index("dep")
    n_col = lax.axis_size("col")
    contract = (((0,), (0,)), ((), ()))
    transposed = (((1,), (1,)), ((), ()))
    pair = [(0, 1), (1, 0)]

    def gather_col(block):
        return lax.all_to_all(jnp.tile(block, (n_col, 1)), "col", 0, 0, tiled=True)

    partner_tokens = lax.ppermute(tokens, "dep", pair)
    gathered = gather_col(tokens)
    first = jnp.dot(gathered, gate_weight, preferred_element_type=jnp.float32)
    second = jnp.dot(gathered, up_weight, preferred_element_type=jnp.float32)
    joined = lax.psum_scatter(
        jnp.concatenate([first, second], axis=1).astype(jnp.bfloat16),
        "row",
        scatter_dimension=0,
        tiled=True,
    )
    gathered_partner = gather_col(partner_tokens)
    joined, gathered_partner = lax.optimization_barrier((joined, gathered_partner))
    joined = joined.astype(jnp.float32)
    gate = joined[:, :width]
    up = joined[:, width:]
    sigma = jax.nn.sigmoid(gate)
    active = gate * sigma
    hidden = (active * up).astype(jnp.bfloat16)
    upstream = cotangent.astype(jnp.float32)
    grad_gate = (upstream * up * sigma * (1.0 + gate * (1.0 - sigma))).astype(jnp.bfloat16)
    grad_up = (upstream * active).astype(jnp.bfloat16)

    gate_own, gate_other = halves(grad_gate, dep, half)
    up_own, up_other = halves(grad_up, dep, half)
    partner_gate, partner_up = jnp.split(
        lax.ppermute(jnp.concatenate([gate_other, up_other], axis=1), "dep", pair), 2, axis=1
    )
    full = lax.all_gather(
        jnp.concatenate(
            [gate_own, up_own, gate_other, up_other, partner_gate, partner_up], axis=1
        ),
        "row", axis=0, tiled=True,
    )

    wg_own, wg_other = halves(gate_weight, dep, half)
    wu_own, wu_other = halves(up_weight, dep, half)
    weights = jnp.concatenate([wg_own, wu_own, wg_other, wu_other], axis=1)
    term = lax.dot_general(
        full[:, :2 * width], weights, transposed, preferred_element_type=jnp.float32
    )
    term = term.astype(jnp.bfloat16).reshape(n_col, -1, term.shape[1])
    term, gathered, gathered_partner = lax.optimization_barrier((term, gathered, gathered_partner))
    parts = lax.all_to_all(term, "col", 0, 0, tiled=True)
    grad_tokens = parts.astype(jnp.float32).sum(axis=0).astype(jnp.bfloat16)

    def weight_grad(own, partner):
        mine = lax.dot_general(gathered, own, contract, preferred_element_type=jnp.float32)
        theirs = lax.dot_general(
            gathered_partner, partner, contract, preferred_element_type=jnp.float32
        )
        return (
            mine.astype(jnp.bfloat16).astype(jnp.float32)
            + theirs.astype(jnp.bfloat16).astype(jnp.float32)
        ).astype(jnp.bfloat16)

    sum_gate = weight_grad(full[:, :half], full[:, 2 * width:2 * width + half])
    sum_up = weight_grad(full[:, half:width], full[:, 2 * width + half:])
    return (hidden, grad_tokens, sum_gate, sum_up)


def solution(mesh):
    return jax.shard_map(
        on_device,
        mesh=mesh,
        in_specs=(
            P(("dep", "col"), "row"),
            P("row", "col"),
            P("row", "col"),
            P(("dep", "row"), "col"),
        ),
        out_specs=(
            P(("dep", "row"), "col"),
            P(("dep", "col"), "row"),
            P("row", ("col", "dep")),
            P("row", ("col", "dep")),
        ),
        check_vma=False,
    )
```

```python
import jax
import jax.numpy as jnp
from jax import lax
from jax.sharding import PartitionSpec as P


def halves(x, dep, half):
    own = lax.dynamic_slice_in_dim(x, dep * half, half, axis=1)
    other = lax.dynamic_slice_in_dim(x, (1 - dep) * half, half, axis=1)
    return own, other


def on_device(tokens, gate_weight, up_weight, cotangent):
    width = gate_weight.shape[1]
    half = width // 2
    dep = lax.axis_index("dep")
    n_col = lax.axis_size("col")
    contract = (((0,), (0,)), ((), ()))
    transposed = (((1,), (1,)), ((), ()))
    pair = [(0, 1), (1, 0)]

    def gather_col(block):
        return lax.all_to_all(jnp.tile(block, (n_col, 1)), "col", 0, 0, tiled=True)

    partner_tokens = lax.ppermute(tokens, "dep", pair)
    gathered = gather_col(tokens)
    first = jnp.dot(gathered, gate_weight, preferred_element_type=jnp.float32)
    second = jnp.dot(gathered, up_weight, preferred_element_type=jnp.float32)
    joined = lax.psum_scatter(
        jnp.concatenate([first, second], axis=1).astype(jnp.bfloat16),
        "row",
        scatter_dimension=0,
        tiled=True,
    )
    gathered_partner = gather_col(partner_tokens)
    joined, gathered_partner = lax.optimization_barrier((joined, gathered_partner))
    joined = joined.astype(jnp.float32)
    gate = joined[:, :width]
    up = joined[:, width:]
    upstream = cotangent.astype(jnp.float32)

    def grads(gate, up, upstream):
        sigma = jax.nn.sigmoid(gate)
        active = gate * sigma
        grad_gate = (upstream * up * sigma * (1.0 + gate * (1.0 - sigma))).astype(jnp.bfloat16)
        return grad_gate, (upstream * active).astype(jnp.bfloat16)

    gate_own, gate_other = halves(gate, dep, half)
    up_own, up_other = halves(up, dep, half)
    up_stream_own, up_stream_other = halves(upstream, dep, half)
    grad_gate_other, grad_up_other = grads(gate_other, up_other, up_stream_other)
    payload = jnp.concatenate([grad_gate_other, grad_up_other], axis=1)
    payload, gate_own, up_own, up_stream_own, gate, up = lax.optimization_barrier(
        (payload, gate_own, up_own, up_stream_own, gate, up)
    )
    partner_gate, partner_up = jnp.split(lax.ppermute(payload, "dep", pair), 2, axis=1)
    grad_gate_own, grad_up_own = grads(gate_own, up_own, up_stream_own)
    hidden = (gate * jax.nn.sigmoid(gate) * up).astype(jnp.bfloat16)
    gate_own, up_own, gate_other, up_other = grad_gate_own, grad_up_own, grad_gate_other, grad_up_other
    full = lax.all_gather(
        jnp.concatenate(
            [gate_own, up_own, gate_other, up_other, partner_gate, partner_up], axis=1
        ),
        "row", axis=0, tiled=True,
    )

    wg_own, wg_other = halves(gate_weight, dep, half)
    wu_own, wu_other = halves(up_weight, dep, half)
    weights = jnp.concatenate([wg_own, wu_own, wg_other, wu_other], axis=1)
    term = lax.dot_general(
        full[:, :2 * width], weights, transposed, preferred_element_type=jnp.float32
    )
    term = term.astype(jnp.bfloat16).reshape(n_col, -1, term.shape[1])
    term, gathered, gathered_partner = lax.optimization_barrier((term, gathered, gathered_partner))
    parts = lax.all_to_all(term, "col", 0, 0, tiled=True)
    grad_tokens = parts.astype(jnp.float32).sum(axis=0).astype(jnp.bfloat16)

    def weight_grad(own, partner):
        mine = lax.dot_general(gathered, own, contract, preferred_element_type=jnp.float32)
        theirs = lax.dot_general(
            gathered_partner, partner, contract, preferred_element_type=jnp.float32
        )
        return (
            mine.astype(jnp.bfloat16).astype(jnp.float32)
            + theirs.astype(jnp.bfloat16).astype(jnp.float32)
        ).astype(jnp.bfloat16)

    sum_gate = weight_grad(full[:, :half], full[:, 2 * width:2 * width + half])
    sum_up = weight_grad(full[:, half:width], full[:, 2 * width + half:])
    return (hidden, grad_tokens, sum_gate, sum_up)


def solution(mesh):
    return jax.shard_map(
        on_device,
        mesh=mesh,
        in_specs=(
            P(("dep", "col"), "row"),
            P("row", "col"),
            P("row", "col"),
            P(("dep", "row"), "col"),
        ),
        out_specs=(
            P(("dep", "row"), "col"),
            P(("dep", "col"), "row"),
            P("row", ("col", "dep")),
            P("row", ("col", "dep")),
        ),
        check_vma=False,
    )
```

```python
import jax
import jax.numpy as jnp
from jax import lax
from jax.experimental.layout import Layout, with_layout_constraint
from jax.sharding import PartitionSpec as P


def halves(x, dep, half):
    own = lax.dynamic_slice_in_dim(x, dep * half, half, axis=1)
    other = lax.dynamic_slice_in_dim(x, (1 - dep) * half, half, axis=1)
    return own, other


def on_device(tokens, gate_weight, up_weight, cotangent):
    width = gate_weight.shape[1]
    half = width // 2
    dep = lax.axis_index("dep")
    n_col = lax.axis_size("col")
    contract = (((0,), (0,)), ((), ()))
    transposed = (((1,), (1,)), ((), ()))
    pair = [(0, 1), (1, 0)]

    def gather_col(block):
        return lax.all_to_all(jnp.tile(block, (n_col, 1)), "col", 0, 0, tiled=True)

    partner_tokens = lax.ppermute(tokens, "dep", pair)
    gathered = gather_col(tokens)
    first = jnp.dot(gathered, gate_weight, preferred_element_type=jnp.float32)
    second = jnp.dot(gathered, up_weight, preferred_element_type=jnp.float32)
    joined = lax.psum_scatter(
        jnp.concatenate([first, second], axis=1).astype(jnp.bfloat16),
        "row",
        scatter_dimension=0,
        tiled=True,
    )
    gathered_partner = gather_col(partner_tokens)
    joined, gathered_partner = lax.optimization_barrier((joined, gathered_partner))
    joined = joined.astype(jnp.float32)
    gate = joined[:, :width]
    up = joined[:, width:]
    upstream = cotangent.astype(jnp.float32)

    def grads(gate, up, upstream):
        sigma = jax.nn.sigmoid(gate)
        active = gate * sigma
        grad_gate = (upstream * up * sigma * (1.0 + gate * (1.0 - sigma))).astype(jnp.bfloat16)
        return grad_gate, (upstream * active).astype(jnp.bfloat16)

    gate_own, gate_other = halves(gate, dep, half)
    up_own, up_other = halves(up, dep, half)
    up_stream_own, up_stream_other = halves(upstream, dep, half)
    grad_gate_other, grad_up_other = grads(gate_other, up_other, up_stream_other)
    payload = jnp.concatenate([grad_gate_other, grad_up_other], axis=1)
    payload, gate_own, up_own, up_stream_own, gate, up = lax.optimization_barrier(
        (payload, gate_own, up_own, up_stream_own, gate, up)
    )
    partner_gate, partner_up = jnp.split(lax.ppermute(payload, "dep", pair), 2, axis=1)
    grad_gate_own, grad_up_own = grads(gate_own, up_own, up_stream_own)
    hidden = (gate * jax.nn.sigmoid(gate) * up).astype(jnp.bfloat16)
    gate_own, up_own, gate_other, up_other = grad_gate_own, grad_up_own, grad_gate_other, grad_up_other
    full = lax.all_gather(
        jnp.concatenate(
            [gate_own, up_own, gate_other, up_other, partner_gate, partner_up], axis=1
        ),
        "row", axis=0, tiled=True,
    )

    wg_own, wg_other = halves(gate_weight, dep, half)
    wu_own, wu_other = halves(up_weight, dep, half)
    weights = with_layout_constraint(
        jnp.concatenate([wg_own, wu_own, wg_other, wu_other], axis=1).T, Layout((0, 1))
    )
    term = jnp.dot(full[:, :2 * width], weights, preferred_element_type=jnp.float32)
    term = term.astype(jnp.bfloat16).reshape(n_col, -1, term.shape[1])
    term, gathered, gathered_partner = lax.optimization_barrier((term, gathered, gathered_partner))
    parts = lax.all_to_all(term, "col", 0, 0, tiled=True)
    grad_tokens = parts.astype(jnp.float32).sum(axis=0).astype(jnp.bfloat16)

    def weight_grad(own, partner):
        mine = lax.dot_general(gathered, own, contract, preferred_element_type=jnp.float32)
        theirs = lax.dot_general(
            gathered_partner, partner, contract, preferred_element_type=jnp.float32
        )
        return (
            mine.astype(jnp.bfloat16).astype(jnp.float32)
            + theirs.astype(jnp.bfloat16).astype(jnp.float32)
        ).astype(jnp.bfloat16)

    sum_gate = weight_grad(full[:, :half], full[:, 2 * width:2 * width + half])
    sum_up = weight_grad(full[:, half:width], full[:, 2 * width + half:])
    return (hidden, grad_tokens, sum_gate, sum_up)


def solution(mesh):
    return jax.shard_map(
        on_device,
        mesh=mesh,
        in_specs=(
            P(("dep", "col"), "row"),
            P("row", "col"),
            P("row", "col"),
            P(("dep", "row"), "col"),
        ),
        out_specs=(
            P(("dep", "row"), "col"),
            P(("dep", "col"), "row"),
            P("row", ("col", "dep")),
            P("row", ("col", "dep")),
        ),
        check_vma=False,
    )
```

```python
import jax
import jax.numpy as jnp
from jax import lax
from jax.sharding import PartitionSpec as P


def halves(x, dep, half):
    own = lax.dynamic_slice_in_dim(x, dep * half, half, axis=1)
    other = lax.dynamic_slice_in_dim(x, (1 - dep) * half, half, axis=1)
    return own, other


def on_device(tokens, gate_weight, up_weight, cotangent):
    width = gate_weight.shape[1]
    half = width // 2
    dep = lax.axis_index("dep")
    n_col = lax.axis_size("col")
    contract = (((0,), (0,)), ((), ()))
    transposed = (((1,), (1,)), ((), ()))
    pair = [(0, 1), (1, 0)]

    def gather_col(block):
        return lax.all_to_all(jnp.tile(block, (n_col, 1)), "col", 0, 0, tiled=True)

    partner_tokens = lax.ppermute(tokens, "dep", pair)
    gathered = gather_col(tokens)
    first = jnp.dot(gathered, gate_weight, preferred_element_type=jnp.float32)
    second = jnp.dot(gathered, up_weight, preferred_element_type=jnp.float32)
    joined = lax.psum_scatter(
        jnp.concatenate([first, second], axis=1).astype(jnp.bfloat16),
        "row",
        scatter_dimension=0,
        tiled=True,
    )
    gathered_partner = gather_col(partner_tokens)
    joined, gathered_partner = lax.optimization_barrier((joined, gathered_partner))
    joined = joined.astype(jnp.float32)
    gate = joined[:, :width]
    up = joined[:, width:]
    upstream = cotangent.astype(jnp.float32)

    def grads(gate, up, upstream):
        sigma = jax.nn.sigmoid(gate)
        active = gate * sigma
        grad_gate = (upstream * up * sigma * (1.0 + gate * (1.0 - sigma))).astype(jnp.bfloat16)
        return grad_gate, (upstream * active).astype(jnp.bfloat16)

    gate_own, gate_other = halves(gate, dep, half)
    up_own, up_other = halves(up, dep, half)
    up_stream_own, up_stream_other = halves(upstream, dep, half)
    grad_gate_other, grad_up_other = grads(gate_other, up_other, up_stream_other)
    payload = jnp.concatenate([grad_gate_other, grad_up_other], axis=1)
    payload, gate_own, up_own, up_stream_own, gate, up = lax.optimization_barrier(
        (payload, gate_own, up_own, up_stream_own, gate, up)
    )
    partner_gate, partner_up = jnp.split(lax.ppermute(payload, "dep", pair), 2, axis=1)
    grad_gate_own, grad_up_own = grads(gate_own, up_own, up_stream_own)
    hidden = (gate * jax.nn.sigmoid(gate) * up).astype(jnp.bfloat16)
    gate_own, up_own, gate_other, up_other = grad_gate_own, grad_up_own, grad_gate_other, grad_up_other
    full = lax.all_gather(
        jnp.stack([
            jnp.concatenate([gate_own, up_own], axis=1),
            jnp.concatenate([gate_other, up_other], axis=1),
            jnp.concatenate([partner_gate, partner_up], axis=1),
        ]),
        "row", axis=1, tiled=True,
    )

    wg_own, wg_other = halves(gate_weight, dep, half)
    wu_own, wu_other = halves(up_weight, dep, half)
    term = lax.dot_general(
        full[0], jnp.concatenate([wg_own, wu_own], axis=1), transposed,
        preferred_element_type=jnp.float32,
    ) + lax.dot_general(
        full[1], jnp.concatenate([wg_other, wu_other], axis=1), transposed,
        preferred_element_type=jnp.float32,
    )
    term = term.astype(jnp.bfloat16).reshape(n_col, -1, term.shape[1])
    term, gathered, gathered_partner = lax.optimization_barrier((term, gathered, gathered_partner))
    parts = lax.all_to_all(term, "col", 0, 0, tiled=True)
    grad_tokens = parts.astype(jnp.float32).sum(axis=0).astype(jnp.bfloat16)

    def weight_grad(own, partner):
        mine = lax.dot_general(gathered, own, contract, preferred_element_type=jnp.float32)
        theirs = lax.dot_general(
            gathered_partner, partner, contract, preferred_element_type=jnp.float32
        )
        return (
            mine.astype(jnp.bfloat16).astype(jnp.float32)
            + theirs.astype(jnp.bfloat16).astype(jnp.float32)
        ).astype(jnp.bfloat16)

    sum_gate = weight_grad(full[0][:, :half], full[2][:, :half])
    sum_up = weight_grad(full[0][:, half:], full[2][:, half:])
    return (hidden, grad_tokens, sum_gate, sum_up)


def solution(mesh):
    return jax.shard_map(
        on_device,
        mesh=mesh,
        in_specs=(
            P(("dep", "col"), "row"),
            P("row", "col"),
            P("row", "col"),
            P(("dep", "row"), "col"),
        ),
        out_specs=(
            P(("dep", "row"), "col"),
            P(("dep", "col"), "row"),
            P("row", ("col", "dep")),
            P("row", ("col", "dep")),
        ),
        check_vma=False,
    )
```

```python
import jax
import jax.numpy as jnp
from jax import lax
from jax.sharding import PartitionSpec as P


def halves(x, dep, half):
    own = lax.dynamic_slice_in_dim(x, dep * half, half, axis=1)
    other = lax.dynamic_slice_in_dim(x, (1 - dep) * half, half, axis=1)
    return own, other


def on_device(tokens, gate_weight, up_weight, cotangent):
    width = gate_weight.shape[1]
    half = width // 2
    dep = lax.axis_index("dep")
    n_col = lax.axis_size("col")
    contract = (((0,), (0,)), ((), ()))
    transposed = (((1,), (1,)), ((), ()))
    pair = [(0, 1), (1, 0)]

    def gather_col(block):
        return lax.all_to_all(jnp.tile(block, (n_col, 1)), "col", 0, 0, tiled=True)

    partner_tokens = lax.ppermute(tokens, "dep", pair)
    gathered = gather_col(tokens)
    first = jnp.dot(gathered, gate_weight, preferred_element_type=jnp.float32)
    second = jnp.dot(gathered, up_weight, preferred_element_type=jnp.float32)
    joined = lax.psum_scatter(
        jnp.concatenate([first, second], axis=1).astype(jnp.bfloat16),
        "row",
        scatter_dimension=0,
        tiled=True,
    )
    gathered_partner = gather_col(partner_tokens)
    joined, gathered_partner = lax.optimization_barrier((joined, gathered_partner))
    gate = joined[:, :width]
    up = joined[:, width:]
    upstream = cotangent

    def grads(gate, up, upstream):
        gate, up, upstream = (x.astype(jnp.float32) for x in (gate, up, upstream))
        sigma = jax.nn.sigmoid(gate)
        active = gate * sigma
        grad_gate = (upstream * up * sigma * (1.0 + gate * (1.0 - sigma))).astype(jnp.bfloat16)
        return grad_gate, (upstream * active).astype(jnp.bfloat16)

    gate_own, gate_other = halves(gate, dep, half)
    up_own, up_other = halves(up, dep, half)
    up_stream_own, up_stream_other = halves(upstream, dep, half)
    grad_gate_other, grad_up_other = grads(gate_other, up_other, up_stream_other)
    payload = jnp.concatenate([grad_gate_other, grad_up_other], axis=1)
    payload, gate_own, up_own, up_stream_own, gate, up = lax.optimization_barrier(
        (payload, gate_own, up_own, up_stream_own, gate, up)
    )
    partner_gate, partner_up = jnp.split(lax.ppermute(payload, "dep", pair), 2, axis=1)
    grad_gate_own, grad_up_own = grads(gate_own, up_own, up_stream_own)
    gate, up = gate.astype(jnp.float32), up.astype(jnp.float32)
    hidden = (gate * jax.nn.sigmoid(gate) * up).astype(jnp.bfloat16)
    gate_own, up_own, gate_other, up_other = grad_gate_own, grad_up_own, grad_gate_other, grad_up_other
    full = lax.all_gather(
        jnp.concatenate(
            [gate_own, up_own, gate_other, up_other, partner_gate, partner_up], axis=1
        ),
        "row", axis=0, tiled=True,
    )

    wg_own, wg_other = halves(gate_weight, dep, half)
    wu_own, wu_other = halves(up_weight, dep, half)
    weights = jnp.concatenate([wg_own, wu_own, wg_other, wu_other], axis=1)
    term = lax.dot_general(
        full[:, :2 * width], weights, transposed, preferred_element_type=jnp.float32
    )
    term = term.astype(jnp.bfloat16).reshape(n_col, -1, term.shape[1])
    term, gathered, gathered_partner = lax.optimization_barrier((term, gathered, gathered_partner))
    parts = lax.all_to_all(term, "col", 0, 0, tiled=True)
    grad_tokens = parts.astype(jnp.float32).sum(axis=0).astype(jnp.bfloat16)

    def weight_grad(own, partner):
        mine = lax.dot_general(gathered, own, contract, preferred_element_type=jnp.float32)
        theirs = lax.dot_general(
            gathered_partner, partner, contract, preferred_element_type=jnp.float32
        )
        return (
            mine.astype(jnp.bfloat16).astype(jnp.float32)
            + theirs.astype(jnp.bfloat16).astype(jnp.float32)
        ).astype(jnp.bfloat16)

    sum_gate = weight_grad(full[:, :half], full[:, 2 * width:2 * width + half])
    sum_up = weight_grad(full[:, half:width], full[:, 2 * width + half:])
    return (hidden, grad_tokens, sum_gate, sum_up)


def solution(mesh):
    return jax.shard_map(
        on_device,
        mesh=mesh,
        in_specs=(
            P(("dep", "col"), "row"),
            P("row", "col"),
            P("row", "col"),
            P(("dep", "row"), "col"),
        ),
        out_specs=(
            P(("dep", "row"), "col"),
            P(("dep", "col"), "row"),
            P("row", ("col", "dep")),
            P("row", ("col", "dep")),
        ),
        check_vma=False,
    )
```
